512 devices in a mesh: obs: 32 (over y, z_lo), gr: 4 (over x), gc: 4 (over z_hi, core).
Axes of the slice: x: 4, y: 8, z: 8 (z_hi: 2, z_lo: 4; z = z_hi * 4 + z_lo), core: 2. Of those that a mesh axis runs over, the one named last changes fastest.
Arguments:
- legendre: float32 [4, 256, 8192], P(None, 'obs'), may hold values from -6 to 6
- longitude: float32 [4, 256], P(None, 'obs'), may hold values from -3.140625 to 3.140625
- orders: int32 [8192], replicated, may hold values from 0 to 360, as said below
- whitening: float32 [4, 256, 256], replicated, as said below
Outputs:
- normal: float32 [16384, 16384], P('obs', ('gr', 'gc'))
The draws below stay inside these ranges and needn't reach their ends.
Inputs may be any that keep to these rules, and one draw needn't show every extreme that they name: The orders of 8192 degree-order pairs that follow one another cyclically in the order-major ordering of a degree-360 field (order m holds degrees m to 360); the run passes from the last pair, of order 360, to the first, of order 0, so the orders rise, fall once from 360 to 0, and rise again. Each arc's whitening matrix is lower triangular with a positive diagonal.
All inputs are finite; a program needn't handle non-finite values.
Results may differ from the reference program's by a relative error of at most 0.0003.
Values sent between devices are 32-bit elements; how exact they have to be, the bound alone decides.
No kernel may reach another device: no remote copies, remote signals or barrier semaphores. Data moves between devices by JAX's collectives and lax.ppermute only.
A program may use at most 64 MiB of HBM per device.

```python
import math
import jax
import jax.numpy as jnp
from jax import lax

PAIRS = 8192
NMAX = 360
ARC = 256
ARCS = 4


def draw_orders(key, part):
    total_pairs = (NMAX + 1) * (NMAX + 2) // 2
    offset = jax.random.randint(key, (), total_pairs - PAIRS + 1, total_pairs, dtype=jnp.int32)
    position = (offset + jnp.arange(PAIRS, dtype=jnp.int32)) % total_pairs
    levels = jnp.arange(1, NMAX + 1, dtype=jnp.int32)
    starts = levels * (NMAX + 1) - levels * (levels - 1) // 2
    return jnp.sum((starts[None, :] <= position[:, None]).astype(jnp.int32), axis=1).astype(jnp.int32)


def draw_whitening(key, part):
    first_key, second_key = jax.random.split(jax.random.fold_in(key, 11))
    diagonal = jnp.exp(jax.random.uniform(first_key, (ARCS, ARC), jnp.float32, math.log(0.5), math.log(2.0)))
    below = jax.random.normal(second_key, (ARCS, ARC, ARC), jnp.float32) * (0.6 / math.sqrt(ARC))
    rows_index = jnp.arange(ARC)[:, None]
    cols_index = jnp.arange(ARC)[None, :]
    lower = (cols_index < rows_index).astype(jnp.float32)
    unit = (cols_index == rows_index).astype(jnp.float32)
    matrix = below * lower[None] + diagonal[:, :, None] * unit[None]
    return (matrix * (1.0 / math.sqrt(ARCS * ARC))).astype(jnp.float32)


def level_of(own_key, extent, cuts, low, top_value):
    def one(dim, shards_of):
        draws = jax.random.uniform(jax.random.fold_in(jax.random.fold_in(own_key, 6), dim), (shards_of,), jnp.float32, low / len(cuts), top_value / len(cuts))
        return jnp.repeat(jnp.exp(draws), extent[dim] // shards_of).reshape((-1,) + (1,) * (len(extent) - dim - 1))

    gain = one(*cuts[0])
    for cut in cuts[1:]:
        gain = gain * one(*cut)
    return gain


def centred(stream_key, extent, width, bound, cuts=(), held_as=jnp.bfloat16):
    factor_of = level_of(stream_key, extent, cuts, -0.22, 0.18) if cuts else 1.0
    entries = jax.random.normal(stream_key, extent, jnp.float32) * width * factor_of
    return jnp.minimum(jnp.maximum(entries, -bound), bound).astype(held_as)


def setup_inputs(seed: int = 0) -> dict:
    key_of = jax.random.split(jax.random.key(seed), 5)
    return {
        "legendre": centred(key_of[0], (ARCS, ARC, PAIRS), 1.0, 6.0, ((1, 32),), jnp.float32),
        "longitude": jnp.clip(jax.random.uniform(key_of[1], (ARCS, ARC), jnp.float32, -3.140625, 3.140625), -3.140625, 3.140625),
        "orders": draw_orders(jax.random.fold_in(key_of[4], 71), 0),
        "whitening": draw_whitening(jax.random.fold_in(key_of[4], 71), 0),
    }


highest = lax.Precision.HIGHEST


def reference(legendre, longitude, orders, whitening):
    order_values = orders.astype(jnp.float32)
    pieces = []
    for arc_index in range(ARCS):
        angles = longitude[arc_index][:, None] * order_values[None, :]
        values = legendre[arc_index]
        design = jnp.stack([values * jnp.cos(angles), values * jnp.sin(angles)], axis=-1).reshape(ARC, 2 * PAIRS)
        pieces.append(jnp.dot(whitening[arc_index], design, precision=highest))
    whitened = jnp.concatenate(pieces, axis=0)
    return jnp.dot(whitened.T, whitened, precision=highest)
```

```python
import jax
import jax.numpy as jnp
from jax import lax
from jax.sharding import PartitionSpec as P

highest = lax.Precision.HIGHEST
LANES = 128


def trig_design(values, angles):
    stacked = jnp.stack([values * jnp.cos(angles), values * jnp.sin(angles)], axis=-1)
    return stacked.reshape(values.shape[:-1] + (2 * values.shape[-1],))


def shards(legendre, longitude, orders, whitening):
    arcs, epochs_local, pairs_total = legendre.shape
    obs_count = lax.axis_size("obs")
    grid_count = lax.axis_size(("gr", "gc"))
    grid_position = lax.axis_index(("gr", "gc"))
    obs_position = lax.axis_index("obs")
    row_pairs = pairs_total // obs_count
    col_pairs = pairs_total // grid_count
    order_values = orders.astype(jnp.float32)

    col_values = lax.dynamic_slice_in_dim(legendre, grid_position * col_pairs, col_pairs, 2)
    row_values = legendre.reshape(arcs, epochs_local, obs_count, row_pairs)
    lon_slab = jnp.broadcast_to(longitude[:, :, None], (arcs, epochs_local, LANES))
    payload = jnp.concatenate(
        [
            jnp.broadcast_to(col_values[:, :, None], (arcs, epochs_local, obs_count, col_pairs)),
            row_values,
            jnp.broadcast_to(lon_slab[:, :, None], (arcs, epochs_local, obs_count, LANES)),
        ],
        axis=3,
    )
    payload = jnp.moveaxis(payload, 2, 0)
    arrived = lax.all_to_all(payload, "obs", 0, 0, tiled=True)
    arrived = jnp.moveaxis(arrived, 0, 1).reshape(arcs, obs_count * epochs_local, -1)

    col_all = arrived[:, :, :col_pairs]
    row_all = arrived[:, :, col_pairs : col_pairs + row_pairs]
    lon_all = arrived[:, :, col_pairs + row_pairs]

    col_orders = lax.dynamic_slice_in_dim(order_values, grid_position * col_pairs, col_pairs, 0)
    row_orders = lax.dynamic_slice_in_dim(order_values, obs_position * row_pairs, row_pairs, 0)
    col_design = trig_design(col_all, lon_all[:, :, None] * col_orders)
    row_design = trig_design(row_all, lon_all[:, :, None] * row_orders)

    col_white = jnp.einsum("afe,aec->afc", whitening, col_design, precision=highest)
    row_white = jnp.einsum("afe,aer->afr", whitening, row_design, precision=highest)
    return jnp.einsum("afr,afc->rc", row_white, col_white, precision=highest)


def solution(mesh):
    placed = (P(None, "obs", None), P(None, "obs"), P(), P())
    return jax.shard_map(
        shards, mesh=mesh, in_specs=placed, out_specs=P("obs", ("gr", "gc")), check_vma=False
    )
```

```python
import jax
import jax.numpy as jnp
from jax import lax
from jax.sharding import PartitionSpec as P

high = lax.Precision.HIGH
LANES = 128


def shards(legendre, longitude, orders, whitening):
    arcs, epochs_local, pairs_total = legendre.shape
    obs_count = lax.axis_size("obs")
    grid_count = lax.axis_size(("gr", "gc"))
    grid_position = lax.axis_index(("gr", "gc"))
    obs_position = lax.axis_index("obs")
    row_pairs = pairs_total // obs_count
    col_pairs = pairs_total // grid_count
    width = col_pairs + row_pairs
    epochs = obs_count * epochs_local
    order_values = orders.astype(jnp.float32)

    col_values = lax.dynamic_slice_in_dim(legendre, grid_position * col_pairs, col_pairs, 2)
    row_values = legendre.reshape(arcs, epochs_local, obs_count, row_pairs)
    data = jnp.concatenate(
        [jnp.broadcast_to(col_values[:, :, None], (arcs, epochs_local, obs_count, col_pairs)), row_values],
        axis=3,
    )
    data = jnp.transpose(data, (2, 1, 0, 3)).reshape(obs_count, epochs_local, arcs * width)
    lon_tile = jnp.pad(longitude.T, ((0, 0), (0, LANES - arcs)))
    lon_tile = jnp.broadcast_to(lon_tile[None], (obs_count, epochs_local, LANES))
    payload = jnp.concatenate([data, lon_tile], axis=2)
    arrived = lax.all_to_all(payload, "obs", 0, 0, tiled=True).reshape(epochs, arcs * width + LANES)
    lon_all = arrived[:, arcs * width : arcs * width + arcs]

    col_orders = lax.dynamic_slice_in_dim(order_values, grid_position * col_pairs, col_pairs, 0)
    row_orders = lax.dynamic_slice_in_dim(order_values, obs_position * row_pairs, row_pairs, 0)

    total = None
    for arc in range(arcs):
        block = arrived[:, arc * width : (arc + 1) * width]
        angles = lon_all[:, arc : arc + 1]
        col_values_all = block[:, :col_pairs]
        row_values_all = block[:, col_pairs:]
        col_angles = angles * col_orders
        row_angles = angles * row_orders
        col_design = jnp.concatenate(
            [col_values_all * jnp.cos(col_angles), col_values_all * jnp.sin(col_angles)], axis=1
        )
        row_design = jnp.concatenate(
            [row_values_all * jnp.cos(row_angles), row_values_all * jnp.sin(row_angles)], axis=1
        )
        col_white = jnp.dot(whitening[arc], col_design, precision=high)
        row_white = jnp.dot(whitening[arc], row_design, precision=high)
        part = lax.dot_general(row_white, col_white, (((0,), (0,)), ((), ())), precision=high)
        total = part if total is None else total + part
    halves = []
    for part_rows in (total[:row_pairs], total[row_pairs:]):
        paired = jnp.stack([part_rows[:, :col_pairs], part_rows[:, col_pairs:]], axis=-1)
        halves.append(paired.reshape(row_pairs, 2 * col_pairs))
    return jnp.stack(halves, axis=1).reshape(2 * row_pairs, 2 * col_pairs)


def solution(mesh):
    placed = (P(None, "obs", None), P(None, "obs"), P(), P())
    return jax.shard_map(
        shards, mesh=mesh, in_specs=placed, out_specs=P("obs", ("gr", "gc")), check_vma=False
    )
```

```python
import jax
import jax.numpy as jnp
from jax import lax
from jax.sharding import PartitionSpec as P

high = lax.Precision.HIGH
LANES = 128


def split3(x):
    hi = lax.reduce_precision(x, exponent_bits=8, mantissa_bits=7)
    rest = x - hi
    mid = lax.reduce_precision(rest, exponent_bits=8, mantissa_bits=7)
    return [p.astype(jnp.bfloat16) for p in (hi, mid, rest - mid)]


def permute_exact(x, perm, left=False):
    out = None
    for piece in split3(x):
        if left:
            term = jnp.dot(perm, piece, preferred_element_type=jnp.float32)
        else:
            term = jnp.dot(piece, perm, preferred_element_type=jnp.float32)
        out = term if out is None else out + term
    return out


def col_perm(half):
    src = lax.broadcasted_iota(jnp.int32, (2 * half, 2 * half), 0)
    dst = lax.broadcasted_iota(jnp.int32, (2 * half, 2 * half), 1)
    return (dst == 2 * (src % half) + src // half).astype(jnp.bfloat16)


def row_perm(half):
    dst = lax.broadcasted_iota(jnp.int32, (2 * half, 2 * half), 0)
    src = lax.broadcasted_iota(jnp.int32, (2 * half, 2 * half), 1)
    return (dst == 2 * (src % half) + src // half).astype(jnp.bfloat16)


def shards(legendre, longitude, orders, whitening):
    arcs, epochs_local, pairs_total = legendre.shape
    obs_count = lax.axis_size("obs")
    grid_count = lax.axis_size(("gr", "gc"))
    grid_position = lax.axis_index(("gr", "gc"))
    obs_position = lax.axis_index("obs")
    row_pairs = pairs_total // obs_count
    col_pairs = pairs_total // grid_count
    width = col_pairs + row_pairs
    epochs = obs_count * epochs_local
    order_values = orders.astype(jnp.float32)

    pieces = []
    for arc in range(arcs):
        col_values = lax.dynamic_slice_in_dim(legendre[arc], grid_position * col_pairs, col_pairs, 1)
        pieces.append(jnp.broadcast_to(col_values[None], (obs_count, epochs_local, col_pairs)))
        pieces.append(jnp.transpose(legendre[arc].reshape(epochs_local, obs_count, row_pairs), (1, 0, 2)))
    lon_tile = jnp.pad(longitude.T, ((0, 0), (0, LANES - arcs)))
    pieces.append(jnp.broadcast_to(lon_tile[None], (obs_count, epochs_local, LANES)))
    payload = jnp.concatenate(pieces, axis=2)
    arrived = lax.all_to_all(payload, "obs", 0, 0, tiled=True).reshape(epochs, arcs * width + LANES)
    lon_all = arrived[:, arcs * width : arcs * width + arcs]

    col_orders = lax.dynamic_slice_in_dim(order_values, grid_position * col_pairs, col_pairs, 0)
    row_orders = lax.dynamic_slice_in_dim(order_values, obs_position * row_pairs, row_pairs, 0)

    total = None
    for arc in range(arcs):
        block = arrived[:, arc * width : (arc + 1) * width]
        angles = lon_all[:, arc : arc + 1]
        col_values_all = block[:, :col_pairs]
        row_values_all = block[:, col_pairs:]
        col_angles = angles * col_orders
        row_angles = angles * row_orders
        col_design = jnp.concatenate(
            [col_values_all * jnp.cos(col_angles), col_values_all * jnp.sin(col_angles)], axis=1
        )
        row_design = jnp.concatenate(
            [row_values_all * jnp.cos(row_angles), row_values_all * jnp.sin(row_angles)], axis=1
        )
        col_white = jnp.dot(whitening[arc], col_design, precision=high)
        row_white = jnp.dot(whitening[arc], row_design, precision=high)
        part = lax.dot_general(row_white, col_white, (((0,), (0,)), ((), ())), precision=high)
        total = part if total is None else total + part
    return permute_exact(permute_exact(total, col_perm(col_pairs)), row_perm(row_pairs), left=True)

def solution(mesh):
    placed = (P(None, "obs", None), P(None, "obs"), P(), P())
    return jax.shard_map(
        shards, mesh=mesh, in_specs=placed, out_specs=P("obs", ("gr", "gc")), check_vma=False
    )
```

```python
import jax
import jax.numpy as jnp
from jax import lax
from jax.sharding import PartitionSpec as P

high = lax.Precision.HIGH
LANES = 128


def split3(x):
    hi = lax.reduce_precision(x, exponent_bits=8, mantissa_bits=7)
    rest = x - hi
    mid = lax.reduce_precision(rest, exponent_bits=8, mantissa_bits=7)
    return [p.astype(jnp.bfloat16) for p in (hi, mid, rest - mid)]


def permute_exact(x, perm, left=False):
    out = None
    for piece in split3(x):
        if left:
            term = jnp.dot(perm, piece, preferred_element_type=jnp.float32)
        else:
            term = jnp.dot(piece, perm, preferred_element_type=jnp.float32)
        out = term if out is None else out + term
    return out


def col_perm(half):
    src = lax.broadcasted_iota(jnp.int32, (2 * half, 2 * half), 0)
    dst = lax.broadcasted_iota(jnp.int32, (2 * half, 2 * half), 1)
    return (dst == 2 * (src % half) + src // half).astype(jnp.bfloat16)


def row_perm(half):
    dst = lax.broadcasted_iota(jnp.int32, (2 * half, 2 * half), 0)
    src = lax.broadcasted_iota(jnp.int32, (2 * half, 2 * half), 1)
    return (dst == 2 * (src % half) + src // half).astype(jnp.bfloat16)


def shards(legendre, longitude, orders, whitening):
    arcs, epochs_local, pairs_total = legendre.shape
    obs_count = lax.axis_size("obs")
    grid_count = lax.axis_size(("gr", "gc"))
    grid_position = lax.axis_index(("gr", "gc"))
    obs_position = lax.axis_index("obs")
    row_pairs = pairs_total // obs_count
    col_pairs = pairs_total // grid_count
    epochs = obs_count * epochs_local
    order_values = orders.astype(jnp.float32)

    core = grid_position % 2
    half_rows = row_pairs // 2
    width = col_pairs + half_rows
    pieces = []
    for arc in range(arcs):
        col_values = lax.dynamic_slice_in_dim(legendre[arc], grid_position * col_pairs, col_pairs, 1)
        pieces.append(jnp.broadcast_to(col_values[None], (obs_count, epochs_local, col_pairs)))
        row_values = legendre[arc].reshape(epochs_local, obs_count, 2, half_rows)
        row_values = lax.dynamic_index_in_dim(row_values, core, 2, keepdims=False)
        pieces.append(jnp.transpose(row_values, (1, 0, 2)))
    lon_tile = jnp.pad(longitude.T, ((0, 0), (0, LANES - arcs)))
    pieces.append(jnp.broadcast_to(lon_tile[None], (obs_count, epochs_local, LANES)))
    payload = jnp.concatenate(pieces, axis=2)
    arrived = lax.all_to_all(payload, "obs", 0, 0, tiled=True).reshape(epochs, arcs * width + LANES)
    lon_all = arrived[:, arcs * width : arcs * width + arcs]

    mine = jnp.stack([arrived[:, arc * width + col_pairs : (arc + 1) * width] for arc in range(arcs)])
    gc_count = lax.axis_size("gc")
    swap = [(k, k ^ 1) for k in range(gc_count)]
    theirs = lax.ppermute(mine, "gc", swap)
    row_all = jnp.where(
        core == 0, jnp.concatenate([mine, theirs], axis=2), jnp.concatenate([theirs, mine], axis=2)
    )

    col_orders = lax.dynamic_slice_in_dim(order_values, grid_position * col_pairs, col_pairs, 0)
    row_orders = lax.dynamic_slice_in_dim(order_values, obs_position * row_pairs, row_pairs, 0)

    total = None
    for arc in range(arcs):
        block = arrived[:, arc * width : (arc + 1) * width]
        angles = lon_all[:, arc : arc + 1]
        col_values_all = block[:, :col_pairs]
        row_values_all = row_all[arc]
        col_angles = angles * col_orders
        row_angles = angles * row_orders
        col_design = jnp.concatenate(
            [col_values_all * jnp.cos(col_angles), col_values_all * jnp.sin(col_angles)], axis=1
        )
        row_design = jnp.concatenate(
            [row_values_all * jnp.cos(row_angles), row_values_all * jnp.sin(row_angles)], axis=1
        )
        col_white = jnp.dot(whitening[arc], col_design, precision=high)
        row_white = jnp.dot(whitening[arc], row_design, precision=high)
        part = lax.dot_general(row_white, col_white, (((0,), (0,)), ((), ())), precision=high)
        total = part if total is None else total + part
    return permute_exact(permute_exact(total, col_perm(col_pairs)), row_perm(row_pairs), left=True)

def solution(mesh):
    placed = (P(None, "obs", None), P(None, "obs"), P(), P())
    return jax.shard_map(
        shards, mesh=mesh, in_specs=placed, out_specs=P("obs", ("gr", "gc")), check_vma=False
    )
```

```python
import jax
import jax.numpy as jnp
from jax import lax
from jax.sharding import PartitionSpec as P

high = lax.Precision.HIGH
LANES = 128


def split3(x):
    hi = lax.reduce_precision(x, exponent_bits=8, mantissa_bits=7)
    rest = x - hi
    mid = lax.reduce_precision(rest, exponent_bits=8, mantissa_bits=7)
    return [p.astype(jnp.bfloat16) for p in (hi, mid, rest - mid)]


def permute_exact(x, perm, left=False):
    out = None
    for piece in split3(x):
        if left:
            term = jnp.dot(perm, piece, preferred_element_type=jnp.float32)
        else:
            term = jnp.dot(piece, perm, preferred_element_type=jnp.float32)
        out = term if out is None else out + term
    return out


def col_perm(half):
    src = lax.broadcasted_iota(jnp.int32, (2 * half, 2 * half), 0)
    dst = lax.broadcasted_iota(jnp.int32, (2 * half, 2 * half), 1)
    return (dst == 2 * (src % half) + src // half).astype(jnp.bfloat16)


def row_perm(half):
    dst = lax.broadcasted_iota(jnp.int32, (2 * half, 2 * half), 0)
    src = lax.broadcasted_iota(jnp.int32, (2 * half, 2 * half), 1)
    return (dst == 2 * (src % half) + src // half).astype(jnp.bfloat16)


SLOTS = 64


def runs_of(block_orders):
    n = block_orders.shape[0]
    change = (block_orders[1:] != block_orders[:-1]).astype(jnp.int32)
    run = jnp.cumsum(jnp.concatenate([jnp.zeros((1,), jnp.int32), change]))
    hot = run[None, :] == lax.broadcasted_iota(jnp.int32, (SLOTS, n), 0)
    value = jnp.max(jnp.where(hot, block_orders[None, :], 0), axis=1).astype(jnp.float32)
    return hot.astype(jnp.bfloat16), value


def shards(legendre, longitude, orders, whitening):
    arcs, epochs_local, pairs_total = legendre.shape
    obs_count = lax.axis_size("obs")
    grid_count = lax.axis_size(("gr", "gc"))
    grid_position = lax.axis_index(("gr", "gc"))
    obs_position = lax.axis_index("obs")
    row_pairs = pairs_total // obs_count
    col_pairs = pairs_total // grid_count
    epochs = obs_count * epochs_local

    core = grid_position % 2
    half_rows = row_pairs // 2
    width = col_pairs + half_rows
    pieces = []
    for arc in range(arcs):
        col_values = lax.dynamic_slice_in_dim(legendre[arc], grid_position * col_pairs, col_pairs, 1)
        pieces.append(jnp.broadcast_to(col_values[None], (obs_count, epochs_local, col_pairs)))
        row_values = legendre[arc].reshape(epochs_local, obs_count, 2, half_rows)
        row_values = lax.dynamic_index_in_dim(row_values, core, 2, keepdims=False)
        pieces.append(jnp.transpose(row_values, (1, 0, 2)))
    lon_tile = jnp.pad(longitude.T, ((0, 0), (0, LANES - arcs)))
    pieces.append(jnp.broadcast_to(lon_tile[None], (obs_count, epochs_local, LANES)))
    payload = jnp.concatenate(pieces, axis=2)
    arrived = lax.all_to_all(payload, "obs", 0, 0, tiled=True).reshape(epochs, arcs * width + LANES)
    lon_all = arrived[:, arcs * width : arcs * width + arcs]

    mine = jnp.stack([arrived[:, arc * width + col_pairs : (arc + 1) * width] for arc in range(arcs)])
    gc_count = lax.axis_size("gc")
    swap = [(k, k ^ 1) for k in range(gc_count)]
    theirs = lax.ppermute(mine, "gc", swap)
    row_all = jnp.where(
        core == 0, jnp.concatenate([mine, theirs], axis=2), jnp.concatenate([theirs, mine], axis=2)
    )

    col_hot, col_value = runs_of(lax.dynamic_slice_in_dim(orders, grid_position * col_pairs, col_pairs, 0))
    row_hot, row_value = runs_of(lax.dynamic_slice_in_dim(orders, obs_position * row_pairs, row_pairs, 0))
    hot = jnp.concatenate(
        [
            jnp.concatenate([col_hot, jnp.zeros((SLOTS, row_pairs), col_hot.dtype)], axis=1),
            jnp.concatenate([jnp.zeros((SLOTS, col_pairs), row_hot.dtype), row_hot], axis=1),
        ],
        axis=0,
    )
    run_values = jnp.concatenate([col_value, row_value])
    run_angles = lon_all.T[:, :, None] * run_values
    cos_all = permute_exact(jnp.cos(run_angles), hot)
    sin_all = permute_exact(jnp.sin(run_angles), hot)

    total = None
    for arc in range(arcs):
        col_values_all = arrived[:, arc * width : arc * width + col_pairs]
        row_values_all = row_all[arc]
        col_design = jnp.concatenate(
            [col_values_all * cos_all[arc, :, :col_pairs], col_values_all * sin_all[arc, :, :col_pairs]], axis=1
        )
        row_design = jnp.concatenate(
            [row_values_all * cos_all[arc, :, col_pairs:], row_values_all * sin_all[arc, :, col_pairs:]], axis=1
        )
        col_white = jnp.dot(whitening[arc], col_design, precision=high)
        row_white = jnp.dot(whitening[arc], row_design, precision=high)
        part = lax.dot_general(row_white, col_white, (((0,), (0,)), ((), ())), precision=high)
        total = part if total is None else total + part
    return permute_exact(permute_exact(total, col_perm(col_pairs)), row_perm(row_pairs), left=True)

def solution(mesh):
    placed = (P(None, "obs", None), P(None, "obs"), P(), P())
    return jax.shard_map(
        shards, mesh=mesh, in_specs=placed, out_specs=P("obs", ("gr", "gc")), check_vma=False
    )
```

```python
import jax
import jax.numpy as jnp
from jax import lax
from jax.sharding import PartitionSpec as P

high = lax.Precision.HIGH
LANES = 128


def split3(x):
    hi = lax.reduce_precision(x, exponent_bits=8, mantissa_bits=7)
    rest = x - hi
    mid = lax.reduce_precision(rest, exponent_bits=8, mantissa_bits=7)
    return [p.astype(jnp.bfloat16) for p in (hi, mid, rest - mid)]


def permute_exact(x, perm, left=False):
    out = None
    for piece in split3(x):
        if left:
            term = jnp.dot(perm, piece, preferred_element_type=jnp.float32)
        else:
            term = jnp.dot(piece, perm, preferred_element_type=jnp.float32)
        out = term if out is None else out + term
    return out


def col_perm(half):
    src = lax.broadcasted_iota(jnp.int32, (2 * half, 2 * half), 0)
    dst = lax.broadcasted_iota(jnp.int32, (2 * half, 2 * half), 1)
    return (dst == 2 * (src % half) + src // half).astype(jnp.bfloat16)


def row_perm(half):
    dst = lax.broadcasted_iota(jnp.int32, (2 * half, 2 * half), 0)
    src = lax.broadcasted_iota(jnp.int32, (2 * half, 2 * half), 1)
    return (dst == 2 * (src % half) + src // half).astype(jnp.bfloat16)


SLOTS = 64


def runs_of(block_orders):
    n = block_orders.shape[0]
    change = (block_orders[1:] != block_orders[:-1]).astype(jnp.int32)
    run = jnp.cumsum(jnp.concatenate([jnp.zeros((1,), jnp.int32), change]))
    hot = run[None, :] == lax.broadcasted_iota(jnp.int32, (SLOTS, n), 0)
    value = jnp.max(jnp.where(hot, block_orders[None, :], 0), axis=1).astype(jnp.float32)
    return hot.astype(jnp.bfloat16), value


def shards(legendre, longitude, orders, whitening):
    arcs, epochs_local, pairs_total = legendre.shape
    obs_count = lax.axis_size("obs")
    grid_count = lax.axis_size(("gr", "gc"))
    grid_position = lax.axis_index(("gr", "gc"))
    obs_position = lax.axis_index("obs")
    row_pairs = pairs_total // obs_count
    col_pairs = pairs_total // grid_count
    epochs = obs_count * epochs_local

    core = grid_position % 2
    half_rows = row_pairs // 2
    width = col_pairs + half_rows
    pieces = []
    for arc in range(arcs):
        col_values = lax.dynamic_slice_in_dim(legendre[arc], grid_position * col_pairs, col_pairs, 1)
        pieces.append(jnp.broadcast_to(col_values[None], (obs_count, epochs_local, col_pairs)))
        row_values = legendre[arc].reshape(epochs_local, obs_count, 2, half_rows)
        row_values = lax.dynamic_index_in_dim(row_values, core, 2, keepdims=False)
        pieces.append(jnp.transpose(row_values, (1, 0, 2)))
    lon_tile = jnp.pad(longitude.T, ((0, 0), (0, LANES - arcs)))
    pieces.append(jnp.broadcast_to(lon_tile[None], (obs_count, epochs_local, LANES)))
    payload = jnp.concatenate(pieces, axis=2)
    arrived = lax.all_to_all(payload, "obs", 0, 0, tiled=True).reshape(epochs, arcs * width + LANES)
    lon_all = arrived[:, arcs * width : arcs * width + arcs]

    mine = jnp.stack([arrived[:, arc * width + col_pairs : (arc + 1) * width] for arc in range(arcs)])
    gc_count = lax.axis_size("gc")
    swap = [(k, k ^ 1) for k in range(gc_count)]
    theirs = lax.ppermute(mine, "gc", swap)
    row_all = jnp.where(
        core == 0, jnp.concatenate([mine, theirs], axis=2), jnp.concatenate([theirs, mine], axis=2)
    )

    col_hot, col_value = runs_of(lax.dynamic_slice_in_dim(orders, grid_position * col_pairs, col_pairs, 0))
    row_hot, row_value = runs_of(lax.dynamic_slice_in_dim(orders, obs_position * row_pairs, row_pairs, 0))
    hot = jnp.concatenate(
        [
            jnp.concatenate([col_hot, jnp.zeros((SLOTS, row_pairs), col_hot.dtype)], axis=1),
            jnp.concatenate([jnp.zeros((SLOTS, col_pairs), row_hot.dtype), row_hot], axis=1),
        ],
        axis=0,
    )
    run_values = jnp.concatenate([col_value, row_value])
    run_angles = lon_all.T[:, :, None] * run_values
    run_cos, run_sin = lax.optimization_barrier((jnp.cos(run_angles), jnp.sin(run_angles)))
    cos_all = permute_exact(run_cos, hot)
    sin_all = permute_exact(run_sin, hot)

    total = None
    for arc in range(arcs):
        col_values_all = arrived[:, arc * width : arc * width + col_pairs]
        row_values_all = row_all[arc]
        col_design = jnp.concatenate(
            [col_values_all * cos_all[arc, :, :col_pairs], col_values_all * sin_all[arc, :, :col_pairs]], axis=1
        )
        row_design = jnp.concatenate(
            [row_values_all * cos_all[arc, :, col_pairs:], row_values_all * sin_all[arc, :, col_pairs:]], axis=1
        )
        col_white = jnp.dot(whitening[arc], col_design, precision=high)
        row_white = jnp.dot(whitening[arc], row_design, precision=high)
        part = lax.dot_general(row_white, col_white, (((0,), (0,)), ((), ())), precision=high)
        total = part if total is None else total + part
    return permute_exact(permute_exact(total, col_perm(col_pairs)), row_perm(row_pairs), left=True)

def solution(mesh):
    placed = (P(None, "obs", None), P(None, "obs"), P(), P())
    return jax.shard_map(
        shards, mesh=mesh, in_specs=placed, out_specs=P("obs", ("gr", "gc")), check_vma=False
    )
```

```python
import jax
import jax.numpy as jnp
from jax import lax
from jax.sharding import PartitionSpec as P

high = lax.Precision.HIGH
LANES = 128


def split3(x):
    hi = lax.reduce_precision(x, exponent_bits=8, mantissa_bits=7)
    rest = x - hi
    mid = lax.reduce_precision(rest, exponent_bits=8, mantissa_bits=7)
    return [p.astype(jnp.bfloat16) for p in (hi, mid, rest - mid)]


def permute_exact(x, perm, left=False):
    out = None
    for piece in split3(x):
        if left:
            term = jnp.einsum("dk,...kc->...dc", perm, piece, preferred_element_type=jnp.float32)
        else:
            term = jnp.einsum("...k,kc->...c", piece, perm, preferred_element_type=jnp.float32)
        out = term if out is None else out + term
    return out


def col_perm(half):
    src = lax.broadcasted_iota(jnp.int32, (2 * half, 2 * half), 0)
    dst = lax.broadcasted_iota(jnp.int32, (2 * half, 2 * half), 1)
    return (dst == 2 * (src % half) + src // half).astype(jnp.bfloat16)


def row_perm(half):
    dst = lax.broadcasted_iota(jnp.int32, (2 * half, 2 * half), 0)
    src = lax.broadcasted_iota(jnp.int32, (2 * half, 2 * half), 1)
    return (dst == 2 * (src % half) + src // half).astype(jnp.bfloat16)


SLOTS = 64


def runs_of(block_orders):
    n = block_orders.shape[0]
    change = (block_orders[1:] != block_orders[:-1]).astype(jnp.int32)
    run = jnp.cumsum(jnp.concatenate([jnp.zeros((1,), jnp.int32), change]))
    hot = run[None, :] == lax.broadcasted_iota(jnp.int32, (SLOTS, n), 0)
    value = jnp.max(jnp.where(hot, block_orders[None, :], 0), axis=1).astype(jnp.float32)
    return hot.astype(jnp.bfloat16), value


def shards(legendre, longitude, orders, whitening):
    arcs, epochs_local, pairs_total = legendre.shape
    obs_count = lax.axis_size("obs")
    grid_count = lax.axis_size(("gr", "gc"))
    grid_position = lax.axis_index(("gr", "gc"))
    obs_position = lax.axis_index("obs")
    row_pairs = pairs_total // obs_count
    col_pairs = pairs_total // grid_count
    epochs = obs_count * epochs_local

    core = grid_position % 2
    half_rows = row_pairs // 2
    width = col_pairs + half_rows
    pieces = []
    for arc in range(arcs):
        col_values = lax.dynamic_slice_in_dim(legendre[arc], grid_position * col_pairs, col_pairs, 1)
        pieces.append(jnp.broadcast_to(col_values[None], (obs_count, epochs_local, col_pairs)))
        row_values = legendre[arc].reshape(epochs_local, obs_count, 2, half_rows)
        row_values = lax.dynamic_index_in_dim(row_values, core, 2, keepdims=False)
        pieces.append(jnp.transpose(row_values, (1, 0, 2)))
    lon_tile = jnp.pad(longitude.T, ((0, 0), (0, LANES - arcs)))
    pieces.append(jnp.broadcast_to(lon_tile[None], (obs_count, epochs_local, LANES)))
    payload = jnp.concatenate(pieces, axis=2)
    arrived = lax.all_to_all(payload, "obs", 0, 0, tiled=True).reshape(epochs, arcs * width + LANES)
    lon_all = arrived[:, arcs * width : arcs * width + arcs]

    mine = jnp.stack([arrived[:, arc * width + col_pairs : (arc + 1) * width] for arc in range(arcs)])
    gc_count = lax.axis_size("gc")
    swap = [(k, k ^ 1) for k in range(gc_count)]
    theirs = lax.ppermute(mine, "gc", swap)
    row_all = jnp.where(
        core == 0, jnp.concatenate([mine, theirs], axis=2), jnp.concatenate([theirs, mine], axis=2)
    )

    col_hot, col_value = runs_of(lax.dynamic_slice_in_dim(orders, grid_position * col_pairs, col_pairs, 0))
    row_hot, row_value = runs_of(lax.dynamic_slice_in_dim(orders, obs_position * row_pairs, row_pairs, 0))
    hot = jnp.concatenate(
        [
            jnp.concatenate([col_hot, jnp.zeros((SLOTS, row_pairs), col_hot.dtype)], axis=1),
            jnp.concatenate([jnp.zeros((SLOTS, col_pairs), row_hot.dtype), row_hot], axis=1),
        ],
        axis=0,
    )
    run_values = jnp.concatenate([col_value, row_value])
    run_angles = lon_all.T[:, :, None] * run_values
    run_cos, run_sin = lax.optimization_barrier((jnp.cos(run_angles), jnp.sin(run_angles)))
    cos_all = permute_exact(run_cos, hot)
    sin_all = permute_exact(run_sin, hot)

    total = None
    for arc in range(arcs):
        col_values_all = arrived[:, arc * width : arc * width + col_pairs]
        row_values_all = row_all[arc]
        col_design = jnp.concatenate(
            [col_values_all * cos_all[arc, :, :col_pairs], col_values_all * sin_all[arc, :, :col_pairs]], axis=1
        )
        row_design = jnp.concatenate(
            [row_values_all * cos_all[arc, :, col_pairs:], row_values_all * sin_all[arc, :, col_pairs:]], axis=1
        )
        col_white = jnp.dot(whitening[arc], col_design, precision=high)
        row_white = jnp.dot(whitening[arc], row_design, precision=high)
        part = lax.dot_general(row_white, col_white, (((0,), (0,)), ((), ())), precision=high)
        total = part if total is None else total + part
    tile = LANES
    rows_out, cols_out = total.shape
    by_cols = total.reshape(rows_out, 2, cols_out // (2 * tile), tile)
    by_cols = jnp.transpose(by_cols, (0, 2, 1, 3)).reshape(rows_out, cols_out // (2 * tile), 2 * tile)
    by_cols = permute_exact(by_cols, col_perm(tile)).reshape(rows_out, cols_out)
    by_rows = by_cols.reshape(2, rows_out // (2 * tile), tile, cols_out)
    by_rows = jnp.transpose(by_rows, (1, 0, 2, 3)).reshape(rows_out // (2 * tile), 2 * tile, cols_out)
    return permute_exact(by_rows, row_perm(tile), left=True).reshape(rows_out, cols_out)

def solution(mesh):
    placed = (P(None, "obs", None), P(None, "obs"), P(), P())
    return jax.shard_map(
        shards, mesh=mesh, in_specs=placed, out_specs=P("obs", ("gr", "gc")), check_vma=False
    )
```

```python
import jax
import jax.numpy as jnp
from jax import lax
from jax.sharding import PartitionSpec as P

high = lax.Precision.HIGH
LANES = 128


def split3(x):
    hi = lax.reduce_precision(x, exponent_bits=8, mantissa_bits=7)
    rest = x - hi
    mid = lax.reduce_precision(rest, exponent_bits=8, mantissa_bits=7)
    return [p.astype(jnp.bfloat16) for p in (hi, mid, rest - mid)]


def permute_exact(x, perm, left=False):
    out = None
    for piece in split3(x):
        if left:
            term = jnp.dot(perm, piece, preferred_element_type=jnp.float32)
        else:
            term = jnp.dot(piece, perm, preferred_element_type=jnp.float32)
        out = term if out is None else out + term
    return out


def col_perm(half):
    src = lax.broadcasted_iota(jnp.int32, (2 * half, 2 * half), 0)
    dst = lax.broadcasted_iota(jnp.int32, (2 * half, 2 * half), 1)
    return (dst == 2 * (src % half) + src // half).astype(jnp.bfloat16)


def row_perm(half):
    dst = lax.broadcasted_iota(jnp.int32, (2 * half, 2 * half), 0)
    src = lax.broadcasted_iota(jnp.int32, (2 * half, 2 * half), 1)
    return (dst == 2 * (src % half) + src // half).astype(jnp.bfloat16)


SLOTS = 64


def runs_of(block_orders):
    n = block_orders.shape[0]
    change = (block_orders[1:] != block_orders[:-1]).astype(jnp.int32)
    run = jnp.cumsum(jnp.concatenate([jnp.zeros((1,), jnp.int32), change]))
    hot = run[None, :] == lax.broadcasted_iota(jnp.int32, (SLOTS, n), 0)
    value = jnp.max(jnp.where(hot, block_orders[None, :], 0), axis=1).astype(jnp.float32)
    return hot.astype(jnp.bfloat16), value


def shards(legendre, longitude, orders, whitening):
    arcs, epochs_local, pairs_total = legendre.shape
    obs_count = lax.axis_size("obs")
    grid_count = lax.axis_size(("gr", "gc"))
    grid_position = lax.axis_index(("gr", "gc"))
    obs_position = lax.axis_index("obs")
    row_pairs = pairs_total // obs_count
    col_pairs = pairs_total // grid_count
    epochs = obs_count * epochs_local

    core = grid_position % 2
    half_rows = row_pairs // 2
    width = col_pairs + half_rows
    pieces = []
    for arc in range(arcs):
        col_values = lax.dynamic_slice_in_dim(legendre[arc], grid_position * col_pairs, col_pairs, 1)
        pieces.append(jnp.broadcast_to(col_values[None], (obs_count, epochs_local, col_pairs)))
        row_values = legendre[arc].reshape(epochs_local, obs_count, 2, half_rows)
        row_values = lax.dynamic_index_in_dim(row_values, core, 2, keepdims=False)
        pieces.append(jnp.transpose(row_values, (1, 0, 2)))
    lon_tile = jnp.pad(longitude.T, ((0, 0), (0, LANES - arcs)))
    pieces.append(jnp.broadcast_to(lon_tile[None], (obs_count, epochs_local, LANES)))
    payload = jnp.concatenate(pieces, axis=2)
    arrived = lax.all_to_all(payload, "obs", 0, 0, tiled=True).reshape(epochs, arcs * width + LANES)
    lon_all = arrived[:, arcs * width : arcs * width + arcs]

    mine = jnp.stack([arrived[:, arc * width + col_pairs : (arc + 1) * width] for arc in range(arcs)])
    gc_count = lax.axis_size("gc")
    swap = [(k, k ^ 1) for k in range(gc_count)]
    theirs = lax.ppermute(mine, "gc", swap)
    row_all = jnp.where(
        core == 0, jnp.concatenate([mine, theirs], axis=2), jnp.concatenate([theirs, mine], axis=2)
    )

    col_hot, col_value = runs_of(lax.dynamic_slice_in_dim(orders, grid_position * col_pairs, col_pairs, 0))
    row_hot, row_value = runs_of(lax.dynamic_slice_in_dim(orders, obs_position * row_pairs, row_pairs, 0))
    hot = jnp.concatenate(
        [
            jnp.concatenate([col_hot, jnp.zeros((SLOTS, row_pairs), col_hot.dtype)], axis=1),
            jnp.concatenate([jnp.zeros((SLOTS, col_pairs), row_hot.dtype), row_hot], axis=1),
        ],
        axis=0,
    )
    run_values = jnp.concatenate([col_value, row_value])
    run_angles = lon_all.T[:, :, None] * run_values
    run_cos, run_sin = lax.optimization_barrier((jnp.cos(run_angles), jnp.sin(run_angles)))
    cos_all = permute_exact(run_cos, hot)
    sin_all = permute_exact(run_sin, hot)

    gram = jnp.einsum("afe,afd->aed", whitening, whitening, precision=high)
    col_designs, row_designs = [], []
    for arc in range(arcs):
        col_values_all = arrived[:, arc * width : arc * width + col_pairs]
        row_values_all = row_all[arc]
        col_designs.append(jnp.concatenate(
            [col_values_all * cos_all[arc, :, :col_pairs], col_values_all * sin_all[arc, :, :col_pairs]], axis=1
        ))
        row_designs.append(jnp.concatenate(
            [row_values_all * cos_all[arc, :, col_pairs:], row_values_all * sin_all[arc, :, col_pairs:]], axis=1
        ))
    col_mixed = jnp.einsum("aed,adc->aec", gram, jnp.stack(col_designs), precision=high)
    total = jnp.einsum("aer,aec->rc", jnp.stack(row_designs), col_mixed, precision=high)
    return permute_exact(permute_exact(total, col_perm(col_pairs)), row_perm(row_pairs), left=True)

def solution(mesh):
    placed = (P(None, "obs", None), P(None, "obs"), P(), P())
    return jax.shard_map(
        shards, mesh=mesh, in_specs=placed, out_specs=P("obs", ("gr", "gc")), check_vma=False
    )
```

```python
import jax
import jax.numpy as jnp
from jax import lax
from jax.experimental import pallas as pl
from jax.experimental.pallas import tpu as pltpu
from jax.sharding import PartitionSpec as P

high = lax.Precision.HIGH
LANES = 128


def split3(x):
    hi = lax.reduce_precision(x, exponent_bits=8, mantissa_bits=7)
    rest = x - hi
    mid = lax.reduce_precision(rest, exponent_bits=8, mantissa_bits=7)
    return [p.astype(jnp.bfloat16) for p in (hi, mid, rest - mid)]


def permute_exact(x, perm, left=False):
    out = None
    for piece in split3(x):
        if left:
            term = jnp.dot(perm, piece, preferred_element_type=jnp.float32)
        else:
            term = jnp.dot(piece, perm, preferred_element_type=jnp.float32)
        out = term if out is None else out + term
    return out


def col_perm(half):
    src = lax.broadcasted_iota(jnp.int32, (2 * half, 2 * half), 0)
    dst = lax.broadcasted_iota(jnp.int32, (2 * half, 2 * half), 1)
    return (dst == 2 * (src % half) + src // half).astype(jnp.bfloat16)


def row_perm(half):
    dst = lax.broadcasted_iota(jnp.int32, (2 * half, 2 * half), 0)
    src = lax.broadcasted_iota(jnp.int32, (2 * half, 2 * half), 1)
    return (dst == 2 * (src % half) + src // half).astype(jnp.bfloat16)


GROUPS = 4


def build_payload(offsets, legendre, lon_tile, peers, col_pairs, half_rows):
    arcs, epochs_local, pairs_total = legendre.shape
    width = col_pairs + half_rows
    per_step = peers // GROUPS
    row_pairs = pairs_total // peers

    def kernel(off_ref, leg_ref, lon_ref, out_ref):
        step = pl.program_id(0)
        col_off = pl.multiple_of(off_ref[0], LANES)
        row_sub = off_ref[1]
        cols = [leg_ref[a, :, pl.ds(col_off, col_pairs)] for a in range(arcs)]
        lon = lon_ref[...]

        def one_peer(j, carry):
            base = pl.multiple_of((step * per_step + j) * row_pairs + row_sub, LANES)
            for a in range(arcs):
                out_ref[j, :, a * width : a * width + col_pairs] = cols[a]
                out_ref[j, :, a * width + col_pairs : (a + 1) * width] = leg_ref[a, :, pl.ds(base, half_rows)]
            out_ref[j, :, arcs * width :] = lon
            return carry

        lax.fori_loop(0, per_step, one_peer, 0)

    return pl.pallas_call(
        kernel,
        out_shape=jax.ShapeDtypeStruct((peers, epochs_local, arcs * width + LANES), legendre.dtype),
        grid=(GROUPS,),
        in_specs=[
            pl.BlockSpec(memory_space=pltpu.SMEM),
            pl.BlockSpec((arcs, epochs_local, pairs_total), lambda i: (0, 0, 0)),
            pl.BlockSpec((epochs_local, LANES), lambda i: (0, 0)),
        ],
        out_specs=pl.BlockSpec((per_step, epochs_local, arcs * width + LANES), lambda i: (i, 0, 0)),
    )(offsets, legendre, lon_tile)


SLOTS = 64


def runs_of(block_orders):
    n = block_orders.shape[0]
    change = (block_orders[1:] != block_orders[:-1]).astype(jnp.int32)
    run = jnp.cumsum(jnp.concatenate([jnp.zeros((1,), jnp.int32), change]))
    hot = run[None, :] == lax.broadcasted_iota(jnp.int32, (SLOTS, n), 0)
    value = jnp.max(jnp.where(hot, block_orders[None, :], 0), axis=1).astype(jnp.float32)
    return hot.astype(jnp.bfloat16), value


def shards(legendre, longitude, orders, whitening):
    arcs, epochs_local, pairs_total = legendre.shape
    obs_count = lax.axis_size("obs")
    grid_count = lax.axis_size(("gr", "gc"))
    grid_position = lax.axis_index(("gr", "gc"))
    obs_position = lax.axis_index("obs")
    row_pairs = pairs_total // obs_count
    col_pairs = pairs_total // grid_count
    epochs = obs_count * epochs_local

    core = grid_position % 2
    half_rows = row_pairs // 2
    width = col_pairs + half_rows
    lon_tile = jnp.pad(longitude.T, ((0, 0), (0, LANES - arcs)))
    offsets = jnp.stack([grid_position * col_pairs, core * half_rows]).astype(jnp.int32)
    payload = build_payload(offsets, legendre, lon_tile, obs_count, col_pairs, half_rows)
    arrived = lax.all_to_all(payload, "obs", 0, 0, tiled=True).reshape(epochs, arcs * width + LANES)
    lon_all = arrived[:, arcs * width : arcs * width + arcs]

    mine = jnp.stack([arrived[:, arc * width + col_pairs : (arc + 1) * width] for arc in range(arcs)])
    gc_count = lax.axis_size("gc")
    swap = [(k, k ^ 1) for k in range(gc_count)]
    theirs = lax.ppermute(mine, "gc", swap)
    row_all = jnp.where(
        core == 0, jnp.concatenate([mine, theirs], axis=2), jnp.concatenate([theirs, mine], axis=2)
    )

    col_hot, col_value = runs_of(lax.dynamic_slice_in_dim(orders, grid_position * col_pairs, col_pairs, 0))
    row_hot, row_value = runs_of(lax.dynamic_slice_in_dim(orders, obs_position * row_pairs, row_pairs, 0))
    hot = jnp.concatenate(
        [
            jnp.concatenate([col_hot, jnp.zeros((SLOTS, row_pairs), col_hot.dtype)], axis=1),
            jnp.concatenate([jnp.zeros((SLOTS, col_pairs), row_hot.dtype), row_hot], axis=1),
        ],
        axis=0,
    )
    run_values = jnp.concatenate([col_value, row_value])
    run_angles = lon_all.T[:, :, None] * run_values
    run_cos, run_sin = lax.optimization_barrier((jnp.cos(run_angles), jnp.sin(run_angles)))
    cos_all = permute_exact(run_cos, hot)
    sin_all = permute_exact(run_sin, hot)

    gram = jnp.einsum("afe,afd->aed", whitening, whitening, precision=high)
    col_designs, row_designs = [], []
    for arc in range(arcs):
        col_values_all = arrived[:, arc * width : arc * width + col_pairs]
        row_values_all = row_all[arc]
        col_designs.append(jnp.concatenate(
            [col_values_all * cos_all[arc, :, :col_pairs], col_values_all * sin_all[arc, :, :col_pairs]], axis=1
        ))
        row_designs.append(jnp.concatenate(
            [row_values_all * cos_all[arc, :, col_pairs:], row_values_all * sin_all[arc, :, col_pairs:]], axis=1
        ))
    col_mixed = jnp.einsum("aed,adc->aec", gram, jnp.stack(col_designs), precision=high)
    total = jnp.einsum("aer,aec->rc", jnp.stack(row_designs), col_mixed, precision=high)
    return permute_exact(permute_exact(total, col_perm(col_pairs)), row_perm(row_pairs), left=True)

def solution(mesh):
    placed = (P(None, "obs", None), P(None, "obs"), P(), P())
    return jax.shard_map(
        shards, mesh=mesh, in_specs=placed, out_specs=P("obs", ("gr", "gc")), check_vma=False
    )
```

```python
import jax
import jax.numpy as jnp
from jax import lax
from jax.experimental import pallas as pl
from jax.experimental.pallas import tpu as pltpu
from jax.sharding import PartitionSpec as P

high = lax.Precision.HIGH
LANES = 128


def split3(x):
    hi = lax.reduce_precision(x, exponent_bits=8, mantissa_bits=7)
    rest = x - hi
    mid = lax.reduce_precision(rest, exponent_bits=8, mantissa_bits=7)
    return [p.astype(jnp.bfloat16) for p in (hi, mid, rest - mid)]


def permute_exact(x, perm, left=False):
    out = None
    for piece in split3(x):
        if left:
            term = jnp.dot(perm, piece, preferred_element_type=jnp.float32)
        else:
            term = jnp.dot(piece, perm, preferred_element_type=jnp.float32)
        out = term if out is None else out + term
    return out


def col_perm(half):
    src = lax.broadcasted_iota(jnp.int32, (2 * half, 2 * half), 0)
    dst = lax.broadcasted_iota(jnp.int32, (2 * half, 2 * half), 1)
    return (dst == 2 * (src % half) + src // half).astype(jnp.bfloat16)


def row_perm(half):
    dst = lax.broadcasted_iota(jnp.int32, (2 * half, 2 * half), 0)
    src = lax.broadcasted_iota(jnp.int32, (2 * half, 2 * half), 1)
    return (dst == 2 * (src % half) + src // half).astype(jnp.bfloat16)


GROUPS = 4


def build_payload(legendre, longitude, peers, col_pairs, half_rows):
    arcs, epochs_local, pairs_total = legendre.shape
    width = col_pairs + half_rows
    per_step = peers // GROUPS
    row_pairs = pairs_total // peers

    def kernel(leg_ref, lon_ref, out_ref):
        step = pl.program_id(0)
        grid_position = lax.axis_index("gr") * lax.axis_size("gc") + lax.axis_index("gc")
        col_off = pl.multiple_of(grid_position * col_pairs, LANES)
        row_sub = (grid_position % 2) * half_rows
        cols = [leg_ref[a, :, pl.ds(col_off, col_pairs)] for a in range(arcs)]
        lon = lon_ref[...]

        def one_peer(j, carry):
            base = pl.multiple_of((step * per_step + j) * row_pairs + row_sub, LANES)
            for a in range(arcs):
                out_ref[j, :, a * width : a * width + col_pairs] = cols[a]
                out_ref[j, :, a * width + col_pairs : (a + 1) * width] = leg_ref[a, :, pl.ds(base, half_rows)]
            out_ref[j, :, arcs * width :] = jnp.zeros((epochs_local, LANES), out_ref.dtype)
            out_ref[j, :arcs, arcs * width : arcs * width + epochs_local] = lon
            return carry

        lax.fori_loop(0, per_step, one_peer, 0)

    return pl.pallas_call(
        kernel,
        out_shape=jax.ShapeDtypeStruct((peers, epochs_local, arcs * width + LANES), legendre.dtype),
        grid=(GROUPS,),
        in_specs=[
            pl.BlockSpec((arcs, epochs_local, pairs_total), lambda i: (0, 0, 0)),
            pl.BlockSpec((arcs, epochs_local), lambda i: (0, 0)),
        ],
        out_specs=pl.BlockSpec((per_step, epochs_local, arcs * width + LANES), lambda i: (i, 0, 0)),
    )(legendre, longitude)


SLOTS = 64


def runs_of(block_orders):
    n = block_orders.shape[0]
    change = (block_orders[1:] != block_orders[:-1]).astype(jnp.int32)
    run = jnp.cumsum(jnp.concatenate([jnp.zeros((1,), jnp.int32), change]))
    hot = run[None, :] == lax.broadcasted_iota(jnp.int32, (SLOTS, n), 0)
    value = jnp.max(jnp.where(hot, block_orders[None, :], 0), axis=1).astype(jnp.float32)
    return hot.astype(jnp.bfloat16), value


def shards(legendre, longitude, orders, whitening):
    arcs, epochs_local, pairs_total = legendre.shape
    obs_count = lax.axis_size("obs")
    grid_count = lax.axis_size(("gr", "gc"))
    grid_position = lax.axis_index(("gr", "gc"))
    obs_position = lax.axis_index("obs")
    row_pairs = pairs_total // obs_count
    col_pairs = pairs_total // grid_count
    epochs = obs_count * epochs_local

    core = grid_position % 2
    half_rows = row_pairs // 2
    width = col_pairs + half_rows
    payload = build_payload(legendre, longitude, obs_count, col_pairs, half_rows)
    arrived = lax.all_to_all(payload, "obs", 0, 0, tiled=True)
    lon_all = jnp.transpose(arrived[:, :arcs, arcs * width : arcs * width + epochs_local], (1, 0, 2))
    lon_all = lon_all.reshape(arcs, epochs)
    arrived = arrived.reshape(epochs, arcs * width + LANES)

    mine = jnp.stack([arrived[:, arc * width + col_pairs : (arc + 1) * width] for arc in range(arcs)])
    gc_count = lax.axis_size("gc")
    swap = [(k, k ^ 1) for k in range(gc_count)]
    theirs = lax.ppermute(mine, "gc", swap)
    row_all = jnp.where(
        core == 0, jnp.concatenate([mine, theirs], axis=2), jnp.concatenate([theirs, mine], axis=2)
    )

    col_hot, col_value = runs_of(lax.dynamic_slice_in_dim(orders, grid_position * col_pairs, col_pairs, 0))
    row_hot, row_value = runs_of(lax.dynamic_slice_in_dim(orders, obs_position * row_pairs, row_pairs, 0))
    hot = jnp.concatenate(
        [
            jnp.concatenate([col_hot, jnp.zeros((SLOTS, row_pairs), col_hot.dtype)], axis=1),
            jnp.concatenate([jnp.zeros((SLOTS, col_pairs), row_hot.dtype), row_hot], axis=1),
        ],
        axis=0,
    )
    run_values = jnp.concatenate([col_value, row_value])
    run_angles = lon_all[:, :, None] * run_values
    run_cos, run_sin = lax.optimization_barrier((jnp.cos(run_angles), jnp.sin(run_angles)))
    cos_all = permute_exact(run_cos, hot)
    sin_all = permute_exact(run_sin, hot)

    gram = jnp.einsum("afe,afd->aed", whitening, whitening, precision=high)
    col_designs, row_designs = [], []
    for arc in range(arcs):
        col_values_all = arrived[:, arc * width : arc * width + col_pairs]
        row_values_all = row_all[arc]
        col_designs.append(jnp.concatenate(
            [col_values_all * cos_all[arc, :, :col_pairs], col_values_all * sin_all[arc, :, :col_pairs]], axis=1
        ))
        row_designs.append(jnp.concatenate(
            [row_values_all * cos_all[arc, :, col_pairs:], row_values_all * sin_all[arc, :, col_pairs:]], axis=1
        ))
    col_mixed = jnp.einsum("aed,adc->aec", gram, jnp.stack(col_designs), precision=high)
    total = jnp.einsum("aer,aec->rc", jnp.stack(row_designs), col_mixed, precision=high)
    return permute_exact(permute_exact(total, col_perm(col_pairs)), row_perm(row_pairs), left=True)

def solution(mesh):
    placed = (P(None, "obs", None), P(None, "obs"), P(), P())
    return jax.shard_map(
        shards, mesh=mesh, in_specs=placed, out_specs=P("obs", ("gr", "gc")), check_vma=False
    )
```

```python
import jax
import jax.numpy as jnp
from jax import lax
from jax.experimental import pallas as pl
from jax.experimental.pallas import tpu as pltpu
from jax.sharding import PartitionSpec as P

high = lax.Precision.HIGH
LANES = 128


def split3(x):
    hi = lax.reduce_precision(x, exponent_bits=8, mantissa_bits=7)
    rest = x - hi
    mid = lax.reduce_precision(rest, exponent_bits=8, mantissa_bits=7)
    return [p.astype(jnp.bfloat16) for p in (hi, mid, rest - mid)]


def permute_exact(x, perm, left=False):
    out = None
    for piece in split3(x):
        if left:
            term = jnp.dot(perm, piece, preferred_element_type=jnp.float32)
        else:
            term = jnp.dot(piece, perm, preferred_element_type=jnp.float32)
        out = term if out is None else out + term
    return out


def col_perm(half):
    src = lax.broadcasted_iota(jnp.int32, (2 * half, 2 * half), 0)
    dst = lax.broadcasted_iota(jnp.int32, (2 * half, 2 * half), 1)
    return (dst == 2 * (src % half) + src // half).astype(jnp.bfloat16)


def row_perm(half):
    dst = lax.broadcasted_iota(jnp.int32, (2 * half, 2 * half), 0)
    src = lax.broadcasted_iota(jnp.int32, (2 * half, 2 * half), 1)
    return (dst == 2 * (src % half) + src // half).astype(jnp.bfloat16)


GROUPS = 4


def build_payload(legendre, longitude, peers, col_pairs, half_rows):
    arcs, epochs_local, pairs_total = legendre.shape
    width = col_pairs + half_rows
    per_step = peers // GROUPS
    row_pairs = pairs_total // peers

    def kernel(leg_ref, lon_ref, out_ref):
        step = pl.program_id(0)
        grid_position = lax.axis_index("gr") * lax.axis_size("gc") + lax.axis_index("gc")
        col_off = pl.multiple_of(grid_position * col_pairs, LANES)
        row_sub = (grid_position % 2) * half_rows
        cols = [leg_ref[a, :, pl.ds(col_off, col_pairs)] for a in range(arcs)]
        lon = lon_ref[...]

        def one_peer(j, carry):
            base = pl.multiple_of((step * per_step + j) * row_pairs + row_sub, LANES)
            for a in range(arcs):
                out_ref[j, :, a * width : a * width + col_pairs] = cols[a]
                out_ref[j, :, a * width + col_pairs : (a + 1) * width] = leg_ref[a, :, pl.ds(base, half_rows)]
            out_ref[j, :, arcs * width :] = jnp.zeros((epochs_local, LANES), out_ref.dtype)
            out_ref[j, :arcs, arcs * width : arcs * width + epochs_local] = lon
            return carry

        lax.fori_loop(0, per_step, one_peer, 0)

    return pl.pallas_call(
        kernel,
        out_shape=jax.ShapeDtypeStruct((peers, epochs_local, arcs * width + LANES), legendre.dtype),
        grid=(GROUPS,),
        in_specs=[
            pl.BlockSpec((arcs, epochs_local, pairs_total), lambda i: (0, 0, 0)),
            pl.BlockSpec((arcs, epochs_local), lambda i: (0, 0)),
        ],
        out_specs=pl.BlockSpec((per_step, epochs_local, arcs * width + LANES), lambda i: (i, 0, 0)),
    )(legendre, longitude)


SLOTS = 64


def runs_of(block_orders):
    n = block_orders.shape[0]
    change = (block_orders[1:] != block_orders[:-1]).astype(jnp.int32)
    run = jnp.cumsum(jnp.concatenate([jnp.zeros((1,), jnp.int32), change]))
    hot = run[None, :] == lax.broadcasted_iota(jnp.int32, (SLOTS, n), 0)
    value = jnp.max(jnp.where(hot, block_orders[None, :], 0), axis=1).astype(jnp.float32)
    return hot.astype(jnp.bfloat16), value


def shards(legendre, longitude, orders, whitening):
    arcs, epochs_local, pairs_total = legendre.shape
    obs_count = lax.axis_size("obs")
    grid_count = lax.axis_size(("gr", "gc"))
    grid_position = lax.axis_index(("gr", "gc"))
    obs_position = lax.axis_index("obs")
    row_pairs = pairs_total // obs_count
    col_pairs = pairs_total // grid_count
    epochs = obs_count * epochs_local

    core = grid_position % 2
    half_rows = row_pairs // 2
    width = col_pairs + half_rows
    payload = build_payload(legendre, longitude, obs_count, col_pairs, half_rows)
    arrived = lax.all_to_all(payload, "obs", 0, 0, tiled=True)
    lon_all = jnp.transpose(arrived[:, :arcs, arcs * width : arcs * width + epochs_local], (1, 0, 2))
    lon_all = lon_all.reshape(arcs, epochs)
    arrived = arrived.reshape(epochs, arcs * width + LANES)

    mine = jnp.stack([arrived[:, arc * width + col_pairs : (arc + 1) * width] for arc in range(arcs)])
    gc_count = lax.axis_size("gc")
    swap = [(k, k ^ 1) for k in range(gc_count)]
    theirs = lax.ppermute(mine, "gc", swap)
    row_all = jnp.where(
        core == 0, jnp.concatenate([mine, theirs], axis=2), jnp.concatenate([theirs, mine], axis=2)
    )

    col_hot, col_value = runs_of(lax.dynamic_slice_in_dim(orders, grid_position * col_pairs, col_pairs, 0))
    row_hot, row_value = runs_of(lax.dynamic_slice_in_dim(orders, obs_position * row_pairs, row_pairs, 0))
    hot = jnp.concatenate(
        [
            jnp.concatenate([col_hot, jnp.zeros((SLOTS, row_pairs), col_hot.dtype)], axis=1),
            jnp.concatenate([jnp.zeros((SLOTS, col_pairs), row_hot.dtype), row_hot], axis=1),
        ],
        axis=0,
    )
    run_values = jnp.concatenate([col_value, row_value])
    run_angles = lon_all[:, :, None] * run_values
    run_cos, run_sin = lax.optimization_barrier((jnp.cos(run_angles), jnp.sin(run_angles)))
    cos_all = permute_exact(run_cos, hot)
    sin_all = permute_exact(run_sin, hot)

    gram = jnp.einsum("afe,afd->aed", whitening, whitening, precision=high)
    col_designs, row_designs = [], []
    for arc in range(arcs):
        col_values_all = arrived[:, arc * width : arc * width + col_pairs]
        row_values_all = row_all[arc]
        col_designs.append(jnp.concatenate(
            [col_values_all * cos_all[arc, :, :col_pairs], col_values_all * sin_all[arc, :, :col_pairs]], axis=1
        ))
        row_designs.append(jnp.concatenate(
            [row_values_all * cos_all[arc, :, col_pairs:], row_values_all * sin_all[arc, :, col_pairs:]], axis=1
        ))
    col_mixed = jnp.einsum("aed,adc->aec", gram, jnp.stack(col_designs), precision=high)
    total = jnp.einsum("aer,aec->rc", jnp.stack(row_designs), col_mixed, precision=high)
    span = 2 * LANES
    by_cols = jnp.concatenate(
        [
            permute_exact(
                jnp.concatenate([total[:, k : k + LANES], total[:, col_pairs + k : col_pairs + k + LANES]], axis=1),
                col_perm(LANES),
            )
            for k in range(0, col_pairs, LANES)
        ],
        axis=1,
    )
    return permute_exact(by_cols, row_perm(row_pairs), left=True)

def solution(mesh):
    placed = (P(None, "obs", None), P(None, "obs"), P(), P())
    return jax.shard_map(
        shards, mesh=mesh, in_specs=placed, out_specs=P("obs", ("gr", "gc")), check_vma=False
    )
```

```python
import jax
import jax.numpy as jnp
from jax import lax
from jax.experimental import pallas as pl
from jax.experimental.pallas import tpu as pltpu
from jax.sharding import PartitionSpec as P

high = lax.Precision.HIGH
LANES = 128


def split3(x):
    hi = lax.reduce_precision(x, exponent_bits=8, mantissa_bits=7)
    rest = x - hi
    mid = lax.reduce_precision(rest, exponent_bits=8, mantissa_bits=7)
    return [p.astype(jnp.bfloat16) for p in (hi, mid, rest - mid)]


def permute_exact(x, perm, left=False):
    pieces = split3(x)
    if left:
        return jnp.einsum(
            "dk,...kc->...dc",
            jnp.concatenate([perm] * 3, axis=1),
            jnp.concatenate(pieces, axis=-2),
            preferred_element_type=jnp.float32,
        )
    return jnp.einsum(
        "...k,kc->...c",
        jnp.concatenate(pieces, axis=-1),
        jnp.concatenate([perm] * 3, axis=0),
        preferred_element_type=jnp.float32,
    )


def col_perm(half):
    src = lax.broadcasted_iota(jnp.int32, (2 * half, 2 * half), 0)
    dst = lax.broadcasted_iota(jnp.int32, (2 * half, 2 * half), 1)
    return (dst == 2 * (src % half) + src // half).astype(jnp.bfloat16)


def row_perm(half):
    dst = lax.broadcasted_iota(jnp.int32, (2 * half, 2 * half), 0)
    src = lax.broadcasted_iota(jnp.int32, (2 * half, 2 * half), 1)
    return (dst == 2 * (src % half) + src // half).astype(jnp.bfloat16)


GROUPS = 4


def build_payload(legendre, longitude, peers, col_pairs, half_rows):
    arcs, epochs_local, pairs_total = legendre.shape
    width = col_pairs + half_rows
    per_step = peers // GROUPS
    row_pairs = pairs_total // peers

    def kernel(leg_ref, lon_ref, out_ref):
        step = pl.program_id(0)
        grid_position = lax.axis_index("gr") * lax.axis_size("gc") + lax.axis_index("gc")
        col_off = pl.multiple_of(grid_position * col_pairs, LANES)
        row_sub = (grid_position % 2) * half_rows
        cols = [leg_ref[a, :, pl.ds(col_off, col_pairs)] for a in range(arcs)]
        lon = lon_ref[...]

        def one_peer(j, carry):
            base = pl.multiple_of((step * per_step + j) * row_pairs + row_sub, LANES)
            for a in range(arcs):
                out_ref[j, :, a * width : a * width + col_pairs] = cols[a]
                out_ref[j, :, a * width + col_pairs : (a + 1) * width] = leg_ref[a, :, pl.ds(base, half_rows)]
            out_ref[j, :, arcs * width :] = jnp.zeros((epochs_local, LANES), out_ref.dtype)
            out_ref[j, :arcs, arcs * width : arcs * width + epochs_local] = lon
            return carry

        lax.fori_loop(0, per_step, one_peer, 0)

    return pl.pallas_call(
        kernel,
        out_shape=jax.ShapeDtypeStruct((peers, epochs_local, arcs * width + LANES), legendre.dtype),
        grid=(GROUPS,),
        in_specs=[
            pl.BlockSpec((arcs, epochs_local, pairs_total), lambda i: (0, 0, 0)),
            pl.BlockSpec((arcs, epochs_local), lambda i: (0, 0)),
        ],
        out_specs=pl.BlockSpec((per_step, epochs_local, arcs * width + LANES), lambda i: (i, 0, 0)),
    )(legendre, longitude)


SLOTS = 64


def runs_of(block_orders):
    n = block_orders.shape[0]
    change = (block_orders[1:] != block_orders[:-1]).astype(jnp.int32)
    run = jnp.cumsum(jnp.concatenate([jnp.zeros((1,), jnp.int32), change]))
    hot = run[None, :] == lax.broadcasted_iota(jnp.int32, (SLOTS, n), 0)
    value = jnp.max(jnp.where(hot, block_orders[None, :], 0), axis=1).astype(jnp.float32)
    return hot.astype(jnp.bfloat16), value


def shards(legendre, longitude, orders, whitening):
    arcs, epochs_local, pairs_total = legendre.shape
    obs_count = lax.axis_size("obs")
    grid_count = lax.axis_size(("gr", "gc"))
    grid_position = lax.axis_index(("gr", "gc"))
    obs_position = lax.axis_index("obs")
    row_pairs = pairs_total // obs_count
    col_pairs = pairs_total // grid_count
    epochs = obs_count * epochs_local

    core = grid_position % 2
    half_rows = row_pairs // 2
    width = col_pairs + half_rows
    payload = build_payload(legendre, longitude, obs_count, col_pairs, half_rows)
    arrived = lax.all_to_all(payload, "obs", 0, 0, tiled=True)
    lon_all = jnp.transpose(arrived[:, :arcs, arcs * width : arcs * width + epochs_local], (1, 0, 2))
    lon_all = lon_all.reshape(arcs, epochs)
    arrived = arrived.reshape(epochs, arcs * width + LANES)

    mine = jnp.stack([arrived[:, arc * width + col_pairs : (arc + 1) * width] for arc in range(arcs)])
    gc_count = lax.axis_size("gc")
    swap = [(k, k ^ 1) for k in range(gc_count)]
    theirs = lax.ppermute(mine, "gc", swap)
    row_all = jnp.where(
        core == 0, jnp.concatenate([mine, theirs], axis=2), jnp.concatenate([theirs, mine], axis=2)
    )

    col_hot, col_value = runs_of(lax.dynamic_slice_in_dim(orders, grid_position * col_pairs, col_pairs, 0))
    row_hot, row_value = runs_of(lax.dynamic_slice_in_dim(orders, obs_position * row_pairs, row_pairs, 0))
    hot = jnp.concatenate(
        [
            jnp.concatenate([col_hot, jnp.zeros((SLOTS, row_pairs), col_hot.dtype)], axis=1),
            jnp.concatenate([jnp.zeros((SLOTS, col_pairs), row_hot.dtype), row_hot], axis=1),
        ],
        axis=0,
    )
    run_values = jnp.concatenate([col_value, row_value])
    run_angles = lon_all[:, :, None] * run_values
    run_cos, run_sin = lax.optimization_barrier((jnp.cos(run_angles), jnp.sin(run_angles)))
    cos_all = permute_exact(run_cos, hot)
    sin_all = permute_exact(run_sin, hot)

    gram = jnp.einsum("afe,afd->aed", whitening, whitening, precision=high)
    col_designs, row_designs = [], []
    for arc in range(arcs):
        col_values_all = arrived[:, arc * width : arc * width + col_pairs]
        row_values_all = row_all[arc]
        col_designs.append(jnp.concatenate(
            [col_values_all * cos_all[arc, :, :col_pairs], col_values_all * sin_all[arc, :, :col_pairs]], axis=1
        ))
        row_designs.append(jnp.concatenate(
            [row_values_all * cos_all[arc, :, col_pairs:], row_values_all * sin_all[arc, :, col_pairs:]], axis=1
        ))
    col_mixed = jnp.einsum("aed,adc->aec", gram, jnp.stack(col_designs), precision=high)
    total = jnp.einsum("aer,aec->rc", jnp.stack(row_designs), col_mixed, precision=high)
    return permute_exact(permute_exact(total, col_perm(col_pairs)), row_perm(row_pairs), left=True)

def solution(mesh):
    placed = (P(None, "obs", None), P(None, "obs"), P(), P())
    return jax.shard_map(
        shards, mesh=mesh, in_specs=placed, out_specs=P("obs", ("gr", "gc")), check_vma=False
    )
```

```python
import jax
import jax.numpy as jnp
from jax import lax
from jax.experimental import pallas as pl
from jax.experimental.pallas import tpu as pltpu
from jax.sharding import PartitionSpec as P

high = lax.Precision.HIGH
LANES = 128


def split3(x):
    hi = lax.reduce_precision(x, exponent_bits=8, mantissa_bits=7)
    rest = x - hi
    mid = lax.reduce_precision(rest, exponent_bits=8, mantissa_bits=7)
    return [p.astype(jnp.bfloat16) for p in (hi, mid, rest - mid)]


def permute_exact(x, perm, left=False):
    pieces = split3(x)
    if left:
        return jnp.einsum(
            "dk,...kc->...dc",
            jnp.concatenate([perm] * 3, axis=1),
            jnp.concatenate(pieces, axis=-2),
            preferred_element_type=jnp.float32,
        )
    return jnp.einsum(
        "...k,kc->...c",
        jnp.concatenate(pieces, axis=-1),
        jnp.concatenate([perm] * 3, axis=0),
        preferred_element_type=jnp.float32,
    )


def col_perm(half):
    src = lax.broadcasted_iota(jnp.int32, (2 * half, 2 * half), 0)
    dst = lax.broadcasted_iota(jnp.int32, (2 * half, 2 * half), 1)
    return (dst == 2 * (src % half) + src // half).astype(jnp.bfloat16)


def row_perm(half):
    dst = lax.broadcasted_iota(jnp.int32, (2 * half, 2 * half), 0)
    src = lax.broadcasted_iota(jnp.int32, (2 * half, 2 * half), 1)
    return (dst == 2 * (src % half) + src // half).astype(jnp.bfloat16)


GROUPS = 4


def build_payload(legendre, longitude, peers, col_pairs, half_rows):
    arcs, epochs_local, pairs_total = legendre.shape
    width = col_pairs + half_rows
    per_step = peers // GROUPS
    row_pairs = pairs_total // peers

    def kernel(leg_ref, lon_ref, out_ref):
        step = pl.program_id(0)
        grid_position = lax.axis_index("gr") * lax.axis_size("gc") + lax.axis_index("gc")
        col_off = pl.multiple_of(grid_position * col_pairs, LANES)
        row_sub = (grid_position % 2) * half_rows
        cols = [leg_ref[a, :, pl.ds(col_off, col_pairs)] for a in range(arcs)]
        lon = lon_ref[...]

        def one_peer(j, carry):
            base = pl.multiple_of((step * per_step + j) * row_pairs + row_sub, LANES)
            for a in range(arcs):
                out_ref[j, :, a * col_pairs : (a + 1) * col_pairs] = cols[a]
                rows_at = arcs * col_pairs + a * half_rows
                out_ref[j, :, rows_at : rows_at + half_rows] = leg_ref[a, :, pl.ds(base, half_rows)]
            out_ref[j, :, arcs * width :] = jnp.zeros((epochs_local, LANES), out_ref.dtype)
            out_ref[j, :arcs, arcs * width : arcs * width + epochs_local] = lon
            return carry

        lax.fori_loop(0, per_step, one_peer, 0)

    return pl.pallas_call(
        kernel,
        out_shape=jax.ShapeDtypeStruct((peers, epochs_local, arcs * width + LANES), legendre.dtype),
        grid=(GROUPS,),
        in_specs=[
            pl.BlockSpec((arcs, epochs_local, pairs_total), lambda i: (0, 0, 0)),
            pl.BlockSpec((arcs, epochs_local), lambda i: (0, 0)),
        ],
        out_specs=pl.BlockSpec((per_step, epochs_local, arcs * width + LANES), lambda i: (i, 0, 0)),
    )(legendre, longitude)


SLOTS = 64


def runs_of(block_orders):
    n = block_orders.shape[0]
    change = (block_orders[1:] != block_orders[:-1]).astype(jnp.int32)
    run = jnp.cumsum(jnp.concatenate([jnp.zeros((1,), jnp.int32), change]))
    hot = run[None, :] == lax.broadcasted_iota(jnp.int32, (SLOTS, n), 0)
    value = jnp.max(jnp.where(hot, block_orders[None, :], 0), axis=1).astype(jnp.float32)
    return hot.astype(jnp.bfloat16), value


def shards(legendre, longitude, orders, whitening):
    arcs, epochs_local, pairs_total = legendre.shape
    obs_count = lax.axis_size("obs")
    grid_count = lax.axis_size(("gr", "gc"))
    grid_position = lax.axis_index(("gr", "gc"))
    obs_position = lax.axis_index("obs")
    row_pairs = pairs_total // obs_count
    col_pairs = pairs_total // grid_count
    epochs = obs_count * epochs_local

    core = grid_position % 2
    half_rows = row_pairs // 2
    width = col_pairs + half_rows
    payload = build_payload(legendre, longitude, obs_count, col_pairs, half_rows)
    arrived = lax.all_to_all(payload, "obs", 0, 0, tiled=True)
    lon_all = jnp.transpose(arrived[:, :arcs, arcs * width : arcs * width + epochs_local], (1, 0, 2))
    lon_all = lon_all.reshape(arcs, epochs)
    arrived = arrived.reshape(epochs, arcs * width + LANES)

    mine = arrived[:, arcs * col_pairs : arcs * width]
    gc_count = lax.axis_size("gc")
    swap = [(k, k ^ 1) for k in range(gc_count)]
    theirs = lax.ppermute(mine, "gc", swap)
    row_all = []
    for arc in range(arcs):
        mine_arc = mine[:, arc * half_rows : (arc + 1) * half_rows]
        theirs_arc = theirs[:, arc * half_rows : (arc + 1) * half_rows]
        row_all.append(jnp.where(
            core == 0, jnp.concatenate([mine_arc, theirs_arc], axis=1), jnp.concatenate([theirs_arc, mine_arc], axis=1)
        ))

    col_hot, col_value = runs_of(lax.dynamic_slice_in_dim(orders, grid_position * col_pairs, col_pairs, 0))
    row_hot, row_value = runs_of(lax.dynamic_slice_in_dim(orders, obs_position * row_pairs, row_pairs, 0))
    hot = jnp.concatenate(
        [
            jnp.concatenate([col_hot, jnp.zeros((SLOTS, row_pairs), col_hot.dtype)], axis=1),
            jnp.concatenate([jnp.zeros((SLOTS, col_pairs), row_hot.dtype), row_hot], axis=1),
        ],
        axis=0,
    )
    run_values = jnp.concatenate([col_value, row_value])
    run_angles = lon_all[:, :, None] * run_values
    run_cos, run_sin = lax.optimization_barrier((jnp.cos(run_angles), jnp.sin(run_angles)))
    cos_all = permute_exact(run_cos, hot)
    sin_all = permute_exact(run_sin, hot)

    gram = jnp.einsum("afe,afd->aed", whitening, whitening, precision=high)
    col_designs, row_designs = [], []
    for arc in range(arcs):
        col_values_all = arrived[:, arc * col_pairs : (arc + 1) * col_pairs]
        row_values_all = row_all[arc]
        col_designs.append(jnp.concatenate(
            [col_values_all * cos_all[arc, :, :col_pairs], col_values_all * sin_all[arc, :, :col_pairs]], axis=1
        ))
        row_designs.append(jnp.concatenate(
            [row_values_all * cos_all[arc, :, col_pairs:], row_values_all * sin_all[arc, :, col_pairs:]], axis=1
        ))
    col_mixed = jnp.einsum("aed,adc->aec", gram, jnp.stack(col_designs), precision=high)
    total = jnp.einsum("aer,aec->rc", jnp.stack(row_designs), col_mixed, precision=high)
    return permute_exact(permute_exact(total, col_perm(col_pairs)), row_perm(row_pairs), left=True)

def solution(mesh):
    placed = (P(None, "obs", None), P(None, "obs"), P(), P())
    return jax.shard_map(
        shards, mesh=mesh, in_specs=placed, out_specs=P("obs", ("gr", "gc")), check_vma=False
    )
```

```python
import jax
import jax.numpy as jnp
from jax import lax
from jax.experimental import pallas as pl
from jax.experimental.pallas import tpu as pltpu
from jax.sharding import PartitionSpec as P

high = lax.Precision.HIGH
LANES = 128


def split3(x):
    hi = lax.reduce_precision(x, exponent_bits=8, mantissa_bits=7)
    rest = x - hi
    mid = lax.reduce_precision(rest, exponent_bits=8, mantissa_bits=7)
    return [p.astype(jnp.bfloat16) for p in (hi, mid, rest - mid)]


def permute_exact(x, perm, left=False):
    pieces = split3(x)
    if left:
        return jnp.einsum(
            "dk,...kc->...dc",
            jnp.concatenate([perm] * 3, axis=1),
            jnp.concatenate(pieces, axis=-2),
            preferred_element_type=jnp.float32,
        )
    return jnp.einsum(
        "...k,kc->...c",
        jnp.concatenate(pieces, axis=-1),
        jnp.concatenate([perm] * 3, axis=0),
        preferred_element_type=jnp.float32,
    )


def col_perm(half):
    src = lax.broadcasted_iota(jnp.int32, (2 * half, 2 * half), 0)
    dst = lax.broadcasted_iota(jnp.int32, (2 * half, 2 * half), 1)
    return (dst == 2 * (src % half) + src // half).astype(jnp.bfloat16)


GROUPS = 4


def build_payload(legendre, longitude, peers, col_pairs, half_rows):
    arcs, epochs_local, pairs_total = legendre.shape
    width = col_pairs + half_rows
    per_step = peers // GROUPS
    row_pairs = pairs_total // peers

    def kernel(leg_ref, lon_ref, out_ref):
        step = pl.program_id(0)
        grid_position = lax.axis_index("gr") * lax.axis_size("gc") + lax.axis_index("gc")
        col_off = pl.multiple_of(grid_position * col_pairs, LANES)
        row_sub = (grid_position % 2) * half_rows
        cols = [leg_ref[a, :, pl.ds(col_off, col_pairs)] for a in range(arcs)]
        lon = lon_ref[...]

        def one_peer(j, carry):
            base = pl.multiple_of((step * per_step + j) * row_pairs + row_sub, LANES)
            for a in range(arcs):
                out_ref[j, :, a * col_pairs : (a + 1) * col_pairs] = cols[a]
                rows_at = arcs * col_pairs + a * half_rows
                out_ref[j, :, rows_at : rows_at + half_rows] = leg_ref[a, :, pl.ds(base, half_rows)]
            out_ref[j, :, arcs * width :] = jnp.zeros((epochs_local, LANES), out_ref.dtype)
            out_ref[j, :arcs, arcs * width : arcs * width + epochs_local] = lon
            return carry

        lax.fori_loop(0, per_step, one_peer, 0)

    return pl.pallas_call(
        kernel,
        out_shape=jax.ShapeDtypeStruct((peers, epochs_local, arcs * width + LANES), legendre.dtype),
        grid=(GROUPS,),
        in_specs=[
            pl.BlockSpec((arcs, epochs_local, pairs_total), lambda i: (0, 0, 0)),
            pl.BlockSpec((arcs, epochs_local), lambda i: (0, 0)),
        ],
        out_specs=pl.BlockSpec((per_step, epochs_local, arcs * width + LANES), lambda i: (i, 0, 0)),
    )(legendre, longitude)


SLOTS = 64


def runs_of(block_orders):
    n = block_orders.shape[0]
    change = (block_orders[1:] != block_orders[:-1]).astype(jnp.int32)
    run = jnp.cumsum(jnp.concatenate([jnp.zeros((1,), jnp.int32), change]))
    hot = run[None, :] == lax.broadcasted_iota(jnp.int32, (SLOTS, n), 0)
    value = jnp.max(jnp.where(hot, block_orders[None, :], 0), axis=1).astype(jnp.float32)
    return hot.astype(jnp.bfloat16), value


def shards(legendre, longitude, orders, whitening):
    arcs, epochs_local, pairs_total = legendre.shape
    obs_count = lax.axis_size("obs")
    grid_count = lax.axis_size(("gr", "gc"))
    grid_position = lax.axis_index(("gr", "gc"))
    obs_position = lax.axis_index("obs")
    row_pairs = pairs_total // obs_count
    col_pairs = pairs_total // grid_count
    epochs = obs_count * epochs_local

    core = grid_position % 2
    half_rows = row_pairs // 2
    width = col_pairs + half_rows
    payload = build_payload(legendre, longitude, obs_count, col_pairs, half_rows)
    arrived = lax.all_to_all(payload, "obs", 0, 0, tiled=True)
    lon_all = jnp.transpose(arrived[:, :arcs, arcs * width : arcs * width + epochs_local], (1, 0, 2))
    lon_all = lon_all.reshape(arcs, epochs)
    arrived = arrived.reshape(epochs, arcs * width + LANES)

    mine = arrived[:, arcs * col_pairs : arcs * width]
    gc_count = lax.axis_size("gc")
    swap = [(k, k ^ 1) for k in range(gc_count)]
    theirs = lax.ppermute(mine, "gc", swap)
    row_all = []
    for arc in range(arcs):
        mine_arc = mine[:, arc * half_rows : (arc + 1) * half_rows]
        theirs_arc = theirs[:, arc * half_rows : (arc + 1) * half_rows]
        row_all.append(jnp.where(
            core == 0, jnp.concatenate([mine_arc, theirs_arc], axis=1), jnp.concatenate([theirs_arc, mine_arc], axis=1)
        ))

    col_hot, col_value = runs_of(lax.dynamic_slice_in_dim(orders, grid_position * col_pairs, col_pairs, 0))
    row_hot, row_value = runs_of(lax.dynamic_slice_in_dim(orders, obs_position * row_pairs, row_pairs, 0))
    hot = jnp.concatenate(
        [
            jnp.concatenate([col_hot, jnp.zeros((SLOTS, row_pairs), col_hot.dtype)], axis=1),
            jnp.concatenate([jnp.zeros((SLOTS, col_pairs), row_hot.dtype), row_hot], axis=1),
        ],
        axis=0,
    )
    run_values = jnp.concatenate([col_value, row_value])
    run_angles = lon_all[:, :, None] * run_values
    run_cos, run_sin = lax.optimization_barrier((jnp.cos(run_angles), jnp.sin(run_angles)))
    cos_all = permute_exact(run_cos, hot)
    sin_all = permute_exact(run_sin, hot)

    gram = jnp.einsum("afe,afd->aed", whitening, whitening, precision=high)
    col_designs, row_designs = [], []
    for arc in range(arcs):
        col_values_all = arrived[:, arc * col_pairs : (arc + 1) * col_pairs]
        row_values_all = row_all[arc]
        col_designs.append(jnp.concatenate(
            [col_values_all * cos_all[arc, :, :col_pairs], col_values_all * sin_all[arc, :, :col_pairs]], axis=1
        ))
        row_designs.append(jnp.concatenate(
            [row_values_all * cos_all[arc, :, col_pairs:], row_values_all * sin_all[arc, :, col_pairs:]], axis=1
        ))
    col_mixed = jnp.einsum("aed,adc->aec", gram, jnp.stack(col_designs), precision=high)
    row_interleaved = permute_exact(jnp.stack(row_designs), col_perm(row_pairs))
    total = jnp.einsum("aer,aec->rc", row_interleaved, col_mixed, precision=high)
    return permute_exact(total, col_perm(col_pairs))

def solution(mesh):
    placed = (P(None, "obs", None), P(None, "obs"), P(), P())
    return jax.shard_map(
        shards, mesh=mesh, in_specs=placed, out_specs=P("obs", ("gr", "gc")), check_vma=False
    )
```

```python
import jax
import jax.numpy as jnp
from jax import lax
from jax.experimental import pallas as pl
from jax.experimental.pallas import tpu as pltpu
from jax.sharding import PartitionSpec as P

high = lax.Precision.HIGH
LANES = 128


def split3(x):
    hi = lax.reduce_precision(x, exponent_bits=8, mantissa_bits=7)
    rest = x - hi
    mid = lax.reduce_precision(rest, exponent_bits=8, mantissa_bits=7)
    return [p.astype(jnp.bfloat16) for p in (hi, mid, rest - mid)]


def permute_exact(x, perm, left=False):
    pieces = split3(x)
    if left:
        return jnp.einsum(
            "dk,...kc->...dc",
            jnp.concatenate([perm] * 3, axis=1),
            jnp.concatenate(pieces, axis=-2),
            preferred_element_type=jnp.float32,
        )
    return jnp.einsum(
        "...k,kc->...c",
        jnp.concatenate(pieces, axis=-1),
        jnp.concatenate([perm] * 3, axis=0),
        preferred_element_type=jnp.float32,
    )


def col_perm(half):
    src = lax.broadcasted_iota(jnp.int32, (2 * half, 2 * half), 0)
    dst = lax.broadcasted_iota(jnp.int32, (2 * half, 2 * half), 1)
    return (dst == 2 * (src % half) + src // half).astype(jnp.bfloat16)


def row_perm(half):
    dst = lax.broadcasted_iota(jnp.int32, (2 * half, 2 * half), 0)
    src = lax.broadcasted_iota(jnp.int32, (2 * half, 2 * half), 1)
    return (dst == 2 * (src % half) + src // half).astype(jnp.bfloat16)


GROUPS = 8


def build_payload(legendre, longitude, peers, col_pairs, half_rows):
    arcs, epochs_local, pairs_total = legendre.shape
    width = col_pairs + half_rows
    per_step = peers // GROUPS
    row_pairs = pairs_total // peers

    def kernel(leg_ref, lon_ref, out_ref):
        step = pl.program_id(0)
        grid_position = lax.axis_index("gr") * lax.axis_size("gc") + lax.axis_index("gc")
        col_off = pl.multiple_of(grid_position * col_pairs, LANES)
        row_sub = (grid_position % 2) * half_rows
        cols = [leg_ref[a, :, pl.ds(col_off, col_pairs)] for a in range(arcs)]
        lon = lon_ref[...]

        def one_peer(j, carry):
            base = pl.multiple_of((step * per_step + j) * row_pairs + row_sub, LANES)
            for a in range(arcs):
                out_ref[j, :, a * col_pairs : (a + 1) * col_pairs] = cols[a]
                rows_at = arcs * col_pairs + a * half_rows
                out_ref[j, :, rows_at : rows_at + half_rows] = leg_ref[a, :, pl.ds(base, half_rows)]
            out_ref[j, :, arcs * width :] = jnp.zeros((epochs_local, LANES), out_ref.dtype)
            out_ref[j, :arcs, arcs * width : arcs * width + epochs_local] = lon
            return carry

        lax.fori_loop(0, per_step, one_peer, 0)

    return pl.pallas_call(
        kernel,
        out_shape=jax.ShapeDtypeStruct((peers, epochs_local, arcs * width + LANES), legendre.dtype),
        grid=(GROUPS,),
        in_specs=[
            pl.BlockSpec((arcs, epochs_local, pairs_total), lambda i: (0, 0, 0)),
            pl.BlockSpec((arcs, epochs_local), lambda i: (0, 0)),
        ],
        out_specs=pl.BlockSpec((per_step, epochs_local, arcs * width + LANES), lambda i: (i, 0, 0)),
    )(legendre, longitude)


SLOTS = 64


def runs_of(block_orders):
    n = block_orders.shape[0]
    change = (block_orders[1:] != block_orders[:-1]).astype(jnp.int32)
    run = jnp.cumsum(jnp.concatenate([jnp.zeros((1,), jnp.int32), change]))
    hot = run[None, :] == lax.broadcasted_iota(jnp.int32, (SLOTS, n), 0)
    value = jnp.max(jnp.where(hot, block_orders[None, :], 0), axis=1).astype(jnp.float32)
    return hot.astype(jnp.bfloat16), value


def shards(legendre, longitude, orders, whitening):
    arcs, epochs_local, pairs_total = legendre.shape
    obs_count = lax.axis_size("obs")
    grid_count = lax.axis_size(("gr", "gc"))
    grid_position = lax.axis_index(("gr", "gc"))
    obs_position = lax.axis_index("obs")
    row_pairs = pairs_total // obs_count
    col_pairs = pairs_total // grid_count
    epochs = obs_count * epochs_local

    core = grid_position % 2
    half_rows = row_pairs // 2
    width = col_pairs + half_rows
    payload = build_payload(legendre, longitude, obs_count, col_pairs, half_rows)
    arrived = lax.all_to_all(payload, "obs", 0, 0, tiled=True)
    lon_all = jnp.transpose(arrived[:, :arcs, arcs * width : arcs * width + epochs_local], (1, 0, 2))
    lon_all = lon_all.reshape(arcs, epochs)
    arrived = arrived.reshape(epochs, arcs * width + LANES)

    mine = arrived[:, arcs * col_pairs : arcs * width]
    gc_count = lax.axis_size("gc")
    swap = [(k, k ^ 1) for k in range(gc_count)]
    theirs = lax.ppermute(mine, "gc", swap)
    row_all = []
    for arc in range(arcs):
        mine_arc = mine[:, arc * half_rows : (arc + 1) * half_rows]
        theirs_arc = theirs[:, arc * half_rows : (arc + 1) * half_rows]
        row_all.append(jnp.where(
            core == 0, jnp.concatenate([mine_arc, theirs_arc], axis=1), jnp.concatenate([theirs_arc, mine_arc], axis=1)
        ))

    col_hot, col_value = runs_of(lax.dynamic_slice_in_dim(orders, grid_position * col_pairs, col_pairs, 0))
    row_hot, row_value = runs_of(lax.dynamic_slice_in_dim(orders, obs_position * row_pairs, row_pairs, 0))
    hot = jnp.concatenate(
        [
            jnp.concatenate([col_hot, jnp.zeros((SLOTS, row_pairs), col_hot.dtype)], axis=1),
            jnp.concatenate([jnp.zeros((SLOTS, col_pairs), row_hot.dtype), row_hot], axis=1),
        ],
        axis=0,
    )
    run_values = jnp.concatenate([col_value, row_value])
    run_angles = lon_all[:, :, None] * run_values
    run_cos, run_sin = lax.optimization_barrier((jnp.cos(run_angles), jnp.sin(run_angles)))
    cos_all = permute_exact(run_cos, hot)
    sin_all = permute_exact(run_sin, hot)

    gram = jnp.einsum("afe,afd->aed", whitening, whitening, precision=high)
    col_designs, row_designs = [], []
    for arc in range(arcs):
        col_values_all = arrived[:, arc * col_pairs : (arc + 1) * col_pairs]
        row_values_all = row_all[arc]
        col_designs.append(jnp.concatenate(
            [col_values_all * cos_all[arc, :, :col_pairs], col_values_all * sin_all[arc, :, :col_pairs]], axis=1
        ))
        row_designs.append(jnp.concatenate(
            [row_values_all * cos_all[arc, :, col_pairs:], row_values_all * sin_all[arc, :, col_pairs:]], axis=1
        ))
    col_mixed = jnp.einsum("aed,adc->aec", gram, jnp.stack(col_designs), precision=high)
    total = jnp.einsum("aer,aec->rc", jnp.stack(row_designs), col_mixed, precision=high)
    return permute_exact(permute_exact(total, col_perm(col_pairs)), row_perm(row_pairs), left=True)

def solution(mesh):
    placed = (P(None, "obs", None), P(None, "obs"), P(), P())
    return jax.shard_map(
        shards, mesh=mesh, in_specs=placed, out_specs=P("obs", ("gr", "gc")), check_vma=False
    )
```
